32 devices in a mesh: scan: 8 (over y, x, core), cuts: 4 (over z).
Axes of the slice: x: 2, y: 2, z: 4, core: 2. Of those that a mesh axis runs over, the one named last changes fastest.
Arguments:
- probe_wave: bfloat16 [2, 512, 512], replicated, may hold values from -6 to 6
- propagator: bfloat16 [2, 512, 512], replicated
- object_slices: float32 [2, 4, 1024, 2048], P(None, 'cuts', 'scan'), may hold values from -4 to 4
- positions: int32 [16, 2], P('scan'), may hold values from 0 to 1536, as said below
- intensities: float32 [16, 512, 512], P('scan'), may hold values from 0 to 2
Outputs:
- object_gradient: float32 [2, 4, 1024, 2048], P(None, 'cuts', 'scan')
The draws below stay inside these ranges and needn't reach their ends.
Inputs may be any that keep to these rules, and one draw needn't show every extreme that they name: `positions`: position j's row lies in [128 * (j // 2), 128 * (j // 2 + 1)); on every index of scan some position's row is the last of that range. Columns lie in 0 to 1536, both ends reached.
All inputs are finite; a program needn't handle non-finite values.
Results may differ from the reference program's by a relative error of at most 0.019.
Values may be sent and summed in bfloat16 or wider, within the bound.
No kernel may reach another device: no remote copies, remote signals or barrier semaphores. Data moves between devices by JAX's collectives and lax.ppermute only.
A program may use at most 128 MiB of HBM per device.

```python
import math
import jax
import jax.numpy as jnp
from jax import lax

P_SIZE = 512
BAND = 128
OW = 2048
POS_DEV = 2
NSL = 4
OH = 1024
NPOS = 16


def draw_propagator(key, part):
    scatter_part = jax.random.normal(key, (2, P_SIZE, P_SIZE), jnp.float32) * (0.3 / P_SIZE ** 0.5)
    identity_part = jnp.eye(P_SIZE, dtype=jnp.float32) * 0.8
    return (scatter_part + jnp.stack([identity_part, jnp.zeros_like(identity_part)])).astype(jnp.bfloat16)


def draw_positions(key, part):
    row_key, column_key = jax.random.split(key)
    serial = jnp.arange(NPOS, dtype=jnp.int32)
    device = serial // POS_DEV
    offset = jax.random.randint(row_key, (NPOS,), 0, BAND, dtype=jnp.int32)
    offset = jnp.where(serial % POS_DEV == device % POS_DEV, BAND - 1, offset)
    column = jax.random.randint(column_key, (NPOS,), 0, OW - P_SIZE + 1, dtype=jnp.int32)
    column = jnp.where(serial == 0, OW - P_SIZE, column)
    column = jnp.where(serial == 1, 0, column)
    return jnp.stack([device * BAND + offset, column], axis=1).astype(jnp.int32)


def shard_levels(key, extent, cuts, smallest, largest):
    factor_of = 1.0
    for dim, shards_of in cuts:
        heights = jax.random.uniform(jax.random.fold_in(jax.random.fold_in(key, 6), dim), (shards_of,), jnp.float32, smallest / len(cuts), largest / len(cuts))
        factor_of = factor_of * jnp.repeat(jnp.exp(heights), extent[dim] // shards_of).reshape((-1,) + (1,) * (len(extent) - 1 - dim))
    return factor_of


def gaussian(own_key, shape, scale, bound, cuts=(), held_as=jnp.bfloat16):
    drawn = scale * jax.random.normal(own_key, shape, jnp.float32)
    if cuts:
        drawn = drawn * shard_levels(own_key, shape, cuts, -0.22, 0.18)
    return jnp.clip(drawn, -bound, bound).astype(held_as)


def setup_inputs(seed: int = 0) -> dict:
    key_of = jax.random.split(jax.random.key(seed), 6)
    probe_wave = gaussian(key_of[0], (2, P_SIZE, P_SIZE), 1.0, 6.0)
    propagator = draw_propagator(jax.random.fold_in(key_of[5], 71), 0)
    object_slices = gaussian(key_of[2], (2, NSL, OH, OW), 0.7, 4.0, ((1, 4), (2, 8)), jnp.float32)
    positions = draw_positions(jax.random.fold_in(key_of[5], 71), 0)
    intensities = jnp.clip(2.0 * jax.random.uniform(key_of[4], (NPOS, P_SIZE, P_SIZE), jnp.float32) ** shard_levels(key_of[4], (NPOS, P_SIZE, P_SIZE), ((0, 8),), -0.2, 0.2), 0.0, 2.0)
    return dict(probe_wave=probe_wave, propagator=propagator, object_slices=object_slices, positions=positions, intensities=intensities)


def complex_product(left_re, left_im, right_re, right_im):
    real_part = jnp.dot(left_re, right_re, preferred_element_type=jnp.float32) - jnp.dot(left_im, right_im, preferred_element_type=jnp.float32)
    imag_part = jnp.dot(left_re, right_im, preferred_element_type=jnp.float32) + jnp.dot(left_im, right_re, preferred_element_type=jnp.float32)
    return jnp.stack([real_part, imag_part])

def dft_table(length):
    serial = jnp.arange(length, dtype=jnp.int32)
    angle_index = serial[:, None] * serial[None, :] % length
    phase_angle = angle_index.astype(jnp.float32) * (2.0 * math.pi / length)
    norm_scale = 1.0 / math.sqrt(length)
    return jnp.stack([jnp.cos(phase_angle) * norm_scale, -jnp.sin(phase_angle) * norm_scale]).astype(jnp.bfloat16)

def forward_section(wave_in, window, propagator):
    mixed_re = wave_in[0] * window[0] - wave_in[1] * window[1]
    mixed_im = wave_in[0] * window[1] + wave_in[1] * window[0]
    mixed = jnp.stack([mixed_re, mixed_im]).astype(jnp.bfloat16)
    halfway = complex_product(propagator[0], propagator[1], mixed[0], mixed[1]).astype(jnp.bfloat16)
    return complex_product(halfway[0], halfway[1], propagator[0].T, propagator[1].T).astype(jnp.bfloat16)

def far_gradient(exit_wave, measured, transform):
    spread = complex_product(transform[0], transform[1], exit_wave[0], exit_wave[1]).astype(jnp.bfloat16)
    farfield = complex_product(spread[0], spread[1], transform[0], transform[1])
    excess = farfield[0] * farfield[0] + farfield[1] * farfield[1] - measured
    residue = (excess[None] * farfield).astype(jnp.bfloat16)
    inverse_im = -transform[1]
    pulled = complex_product(transform[0], inverse_im, residue[0], residue[1]).astype(jnp.bfloat16)
    return complex_product(pulled[0], pulled[1], transform[0], inverse_im).astype(jnp.bfloat16)

def adjoint_section(grad_out, wave_in, window, propagator):
    conj_im = -propagator[1]
    grad_half = complex_product(grad_out[0], grad_out[1], propagator[0], conj_im).astype(jnp.bfloat16)
    grad_mixed = complex_product(propagator[0].T, conj_im.T, grad_half[0], grad_half[1])
    object_re = wave_in[0] * grad_mixed[0] + wave_in[1] * grad_mixed[1]
    object_im = wave_in[0] * grad_mixed[1] - wave_in[1] * grad_mixed[0]
    wave_re = window[0] * grad_mixed[0] + window[1] * grad_mixed[1]
    wave_im = window[0] * grad_mixed[1] - window[1] * grad_mixed[0]
    return (jnp.stack([object_re, object_im]), jnp.stack([wave_re, wave_im]).astype(jnp.bfloat16))

def reference(probe_wave, propagator, object_slices, positions, intensities):
    window_size = probe_wave.shape[1]
    slices = object_slices.shape[1]
    height = object_slices.shape[2]
    width = object_slices.shape[3]
    widened = jnp.concatenate([object_slices, object_slices[:, :, :window_size]], axis=2)
    transform = dft_table(window_size)

    def one_position(gradient_sum, inputs):
        position, measured = inputs
        corner = (jnp.int32(0), jnp.int32(0), position[0].astype(jnp.int32), position[1].astype(jnp.int32))
        windows = lax.dynamic_slice(widened, corner, (2, slices, window_size, window_size))
        waves = []
        wave_now = probe_wave
        for slice_index in range(slices):
            waves.append(wave_now)
            wave_now = forward_section(wave_now, windows[:, slice_index], propagator)
        grad_wave = far_gradient(wave_now, measured, transform)
        object_grads = [None] * slices
        for slice_index in range(slices - 1, -1, -1):
            object_grads[slice_index], grad_wave = adjoint_section(grad_wave, waves[slice_index], windows[:, slice_index], propagator)
        window_grad = jnp.stack(object_grads, axis=1)
        current = lax.dynamic_slice(gradient_sum, corner, (2, slices, window_size, window_size))
        return (lax.dynamic_update_slice(gradient_sum, current + window_grad, corner), None)
    initial = jnp.zeros((2, slices, height + window_size, width), jnp.float32)
    gradient_sum, unused = lax.scan(one_position, initial, (positions, intensities))
    folded = gradient_sum[:, :, :height]
    return folded.at[:, :, :window_size].add(gradient_sum[:, :, height:])
```

```python
import math

import jax
import jax.numpy as jnp
from jax import lax
from jax.sharding import PartitionSpec as P


def passed_along(shard, axis, by):
    devices = lax.axis_size(axis)
    return lax.ppermute(shard, axis, [(i, (i + by) % devices) for i in range(devices)])


def complex_product(left_re, left_im, right_re, right_im):
    real_part = jnp.dot(left_re, right_re, preferred_element_type=jnp.float32) - jnp.dot(
        left_im, right_im, preferred_element_type=jnp.float32
    )
    imag_part = jnp.dot(left_re, right_im, preferred_element_type=jnp.float32) + jnp.dot(
        left_im, right_re, preferred_element_type=jnp.float32
    )
    return jnp.stack([real_part, imag_part])


def dft_table(length):
    serial = jnp.arange(length, dtype=jnp.int32)
    angle_index = serial[:, None] * serial[None, :] % length
    phase_angle = angle_index.astype(jnp.float32) * (2.0 * math.pi / length)
    norm_scale = 1.0 / math.sqrt(length)
    return jnp.stack(
        [jnp.cos(phase_angle) * norm_scale, -jnp.sin(phase_angle) * norm_scale]
    ).astype(jnp.bfloat16)


def forward_section(wave_in, window, propagator):
    mixed_re = wave_in[0] * window[0] - wave_in[1] * window[1]
    mixed_im = wave_in[0] * window[1] + wave_in[1] * window[0]
    mixed = jnp.stack([mixed_re, mixed_im]).astype(jnp.bfloat16)
    halfway = complex_product(propagator[0], propagator[1], mixed[0], mixed[1]).astype(jnp.bfloat16)
    return complex_product(halfway[0], halfway[1], propagator[0].T, propagator[1].T).astype(
        jnp.bfloat16
    )


def far_gradient(exit_wave, measured, transform):
    spread = complex_product(transform[0], transform[1], exit_wave[0], exit_wave[1]).astype(
        jnp.bfloat16
    )
    farfield = complex_product(spread[0], spread[1], transform[0], transform[1])
    excess = farfield[0] * farfield[0] + farfield[1] * farfield[1] - measured
    residue = (excess[None] * farfield).astype(jnp.bfloat16)
    inverse_im = -transform[1]
    pulled = complex_product(transform[0], inverse_im, residue[0], residue[1]).astype(jnp.bfloat16)
    return complex_product(pulled[0], pulled[1], transform[0], inverse_im).astype(jnp.bfloat16)


def adjoint_section(grad_out, wave_in, window, propagator):
    conj_im = -propagator[1]
    grad_half = complex_product(grad_out[0], grad_out[1], propagator[0], conj_im).astype(
        jnp.bfloat16
    )
    grad_mixed = complex_product(propagator[0].T, conj_im.T, grad_half[0], grad_half[1])
    object_re = wave_in[0] * grad_mixed[0] + wave_in[1] * grad_mixed[1]
    object_im = wave_in[0] * grad_mixed[1] - wave_in[1] * grad_mixed[0]
    wave_re = window[0] * grad_mixed[0] + window[1] * grad_mixed[1]
    wave_im = window[0] * grad_mixed[1] - window[1] * grad_mixed[0]
    return (jnp.stack([object_re, object_im]), jnp.stack([wave_re, wave_im]).astype(jnp.bfloat16))


def whole_chain(probe_wave, propagator, windows, measured, transform):
    waves = []
    wave_now = probe_wave
    for window in windows:
        waves.append(wave_now)
        wave_now = forward_section(wave_now, window, propagator)
    grad_wave = far_gradient(wave_now, measured, transform)
    grads = [None] * len(windows)
    for index in range(len(windows) - 1, -1, -1):
        grads[index], grad_wave = adjoint_section(grad_wave, waves[index], windows[index], propagator)
    return jnp.stack(grads)


def pack_rounds(transfers):
    rounds = []
    for item in transfers:
        for members in rounds:
            if all(item[1] != other[1] and item[2] != other[2] for other in members):
                members.append(item)
                break
        else:
            rounds.append([item])
    return rounds


def chosen(options):
    result = jnp.zeros_like(options[0][1])
    for condition, value in options:
        result = jnp.where(condition, value, result)
    return result


def local(probe_wave, propagator, object_slices, positions, intensities):
    window_size = probe_wave.shape[1]
    band_rows = object_slices.shape[2]
    reach = window_size // band_rows
    local_count = positions.shape[0]
    groups = lax.axis_size("scan")
    sections = lax.axis_size("cuts")
    group = lax.axis_index("scan")
    section = lax.axis_index("cuts")
    assert local_count <= sections
    hosts = [(sections - local_count) // 2 + k for k in range(local_count)]
    host_of = jnp.array(hosts, jnp.int32)

    every_position = lax.all_gather(positions, "scan")
    own_band = object_slices[:, 0]
    row_offsets = positions[:, 0] % band_rows

    def pieces_for(target):
        columns = every_position[target % groups, :, 1]
        return jnp.stack(
            [lax.dynamic_slice_in_dim(own_band, columns[k], window_size, axis=2) for k in range(local_count)]
        )

    stacked = [pieces_for(group)]
    for distance in range(1, reach + 1):
        outgoing = pieces_for(group - distance).astype(jnp.bfloat16)
        stacked.append(passed_along(outgoing, "scan", -distance).astype(jnp.float32))
    tall = jnp.concatenate(stacked, axis=2)
    windows_here = jnp.stack(
        [
            lax.dynamic_slice_in_dim(tall[k], row_offsets[k], window_size, axis=1)
            for k in range(local_count)
        ]
    )

    transfers = [
        (k, t, hosts[k]) for t in range(sections) for k in range(local_count) if t != hosts[k]
    ]
    rounds = pack_rounds(transfers)
    is_host = jnp.any(host_of == section)
    hosted = jnp.argmax(host_of == section).astype(jnp.int32)
    arrivals = {}
    for members in rounds:
        send_k = [0] * sections
        for k, sender, receiver in members:
            send_k[sender] = k
        picked = jnp.array(send_k, jnp.int32)[section]
        outgoing = lax.dynamic_index_in_dim(windows_here, picked, 0, keepdims=False)
        incoming = lax.ppermute(
            outgoing.astype(jnp.bfloat16), "cuts", [(m[1], m[2]) for m in members]
        )
        for k, sender, receiver in members:
            arrivals[(k, sender)] = incoming

    windows = []
    own_window = lax.dynamic_index_in_dim(windows_here, hosted, 0, keepdims=False)
    for t in range(sections):
        options = [(section == t, own_window)]
        for k in range(local_count):
            if t != hosts[k]:
                options.append(((hosted == k) & (section != t), arrivals[(k, t)].astype(jnp.float32)))
        windows.append(chosen(options))

    transform = lax.optimization_barrier(dft_table(window_size))
    measured = lax.dynamic_index_in_dim(intensities, hosted, 0, keepdims=False)
    zero_grads = jnp.zeros((sections, 2, window_size, window_size), jnp.float32)
    grads = lax.cond(
        is_host,
        lambda: whole_chain(probe_wave, propagator, windows, measured, transform),
        lambda: zero_grads,
    )

    returns = [(k, hosts[k], t) for t in range(sections - 1, -1, -1) for k in range(local_count) if t != hosts[k]]
    back_rounds = pack_rounds(returns)
    returned = {}
    for members in back_rounds:
        send_t = [0] * sections
        for k, sender, receiver in members:
            send_t[sender] = receiver
        picked = jnp.array(send_t, jnp.int32)[section]
        outgoing = lax.dynamic_index_in_dim(grads, picked, 0, keepdims=False)
        incoming = lax.ppermute(
            outgoing.astype(jnp.bfloat16), "cuts", [(m[1], m[2]) for m in members]
        )
        for k, sender, receiver in members:
            returned[(k, receiver)] = incoming

    own_grad = lax.dynamic_index_in_dim(grads, section, 0, keepdims=False)
    window_grads = []
    for k in range(local_count):
        options = [(section == hosts[k], own_grad)]
        for t in range(sections):
            if t != hosts[k]:
                options.append((section == t, returned[(k, t)].astype(jnp.float32)))
        window_grads.append(chosen(options))

    padded = jnp.zeros((local_count, 2, (reach + 1) * band_rows, window_size), jnp.float32)
    for k in range(local_count):
        padded = padded.at[k].set(
            lax.dynamic_update_slice_in_dim(padded[k], window_grads[k], row_offsets[k], axis=1)
        )

    summed = jnp.zeros_like(own_band)

    def added(total, piece, columns):
        for k in range(local_count):
            current = lax.dynamic_slice_in_dim(total, columns[k], window_size, axis=2)
            total = lax.dynamic_update_slice_in_dim(total, current + piece[k], columns[k], axis=2)
        return total

    summed = added(summed, padded[:, :, :band_rows], every_position[group, :, 1])
    for distance in range(1, reach + 1):
        outgoing = padded[:, :, distance * band_rows : (distance + 1) * band_rows].astype(jnp.bfloat16)
        incoming = passed_along(outgoing, "scan", distance).astype(jnp.float32)
        summed = added(summed, incoming, every_position[(group - distance) % groups, :, 1])
    return summed[:, None]


def solution(mesh):
    in_specs = (P(), P(), P(None, "cuts", "scan", None), P("scan", None), P("scan", None, None))
    out_specs = P(None, "cuts", "scan", None)
    return jax.shard_map(local, mesh=mesh, in_specs=in_specs, out_specs=out_specs, check_vma=False)
```

```python
import math

import jax
import jax.numpy as jnp
from jax import lax
from jax.sharding import PartitionSpec as P


def passed_along(shard, axis, by):
    devices = lax.axis_size(axis)
    return lax.ppermute(shard, axis, [(i, (i + by) % devices) for i in range(devices)])


def complex_product(left_re, left_im, right_re, right_im):
    real_part = jnp.dot(left_re, right_re, preferred_element_type=jnp.float32) - jnp.dot(
        left_im, right_im, preferred_element_type=jnp.float32
    )
    imag_part = jnp.dot(left_re, right_im, preferred_element_type=jnp.float32) + jnp.dot(
        left_im, right_re, preferred_element_type=jnp.float32
    )
    return jnp.stack([real_part, imag_part])


def dft_table(length):
    serial = jnp.arange(length, dtype=jnp.int32)
    angle_index = serial[:, None] * serial[None, :] % length
    phase_angle = angle_index.astype(jnp.float32) * (2.0 * math.pi / length)
    norm_scale = 1.0 / math.sqrt(length)
    return jnp.stack(
        [jnp.cos(phase_angle) * norm_scale, -jnp.sin(phase_angle) * norm_scale]
    ).astype(jnp.bfloat16)


def forward_section(wave_in, window, propagator):
    mixed_re = wave_in[0] * window[0] - wave_in[1] * window[1]
    mixed_im = wave_in[0] * window[1] + wave_in[1] * window[0]
    mixed = jnp.stack([mixed_re, mixed_im]).astype(jnp.bfloat16)
    halfway = complex_product(propagator[0], propagator[1], mixed[0], mixed[1]).astype(jnp.bfloat16)
    return complex_product(halfway[0], halfway[1], propagator[0].T, propagator[1].T).astype(
        jnp.bfloat16
    )


def far_gradient(exit_wave, measured, transform):
    spread = complex_product(transform[0], transform[1], exit_wave[0], exit_wave[1]).astype(
        jnp.bfloat16
    )
    farfield = complex_product(spread[0], spread[1], transform[0], transform[1])
    excess = farfield[0] * farfield[0] + farfield[1] * farfield[1] - measured
    residue = (excess[None] * farfield).astype(jnp.bfloat16)
    inverse_im = -transform[1]
    pulled = complex_product(transform[0], inverse_im, residue[0], residue[1]).astype(jnp.bfloat16)
    return complex_product(pulled[0], pulled[1], transform[0], inverse_im).astype(jnp.bfloat16)


def adjoint_section(grad_out, wave_in, window, propagator):
    conj_im = -propagator[1]
    grad_half = complex_product(grad_out[0], grad_out[1], propagator[0], conj_im).astype(
        jnp.bfloat16
    )
    grad_mixed = complex_product(propagator[0].T, conj_im.T, grad_half[0], grad_half[1])
    object_re = wave_in[0] * grad_mixed[0] + wave_in[1] * grad_mixed[1]
    object_im = wave_in[0] * grad_mixed[1] - wave_in[1] * grad_mixed[0]
    wave_re = window[0] * grad_mixed[0] + window[1] * grad_mixed[1]
    wave_im = window[0] * grad_mixed[1] - window[1] * grad_mixed[0]
    return (jnp.stack([object_re, object_im]), jnp.stack([wave_re, wave_im]).astype(jnp.bfloat16))


def whole_chain(probe_wave, propagator, windows, measured, transform):
    waves = []
    wave_now = probe_wave
    for window in windows:
        waves.append(wave_now)
        wave_now = forward_section(wave_now, window, propagator)
    grad_wave = far_gradient(wave_now, measured, transform)
    grads = [None] * len(windows)
    for index in range(len(windows) - 1, -1, -1):
        grads[index], grad_wave = adjoint_section(grad_wave, waves[index], windows[index], propagator)
    return grads


def chosen(options):
    result = jnp.zeros_like(options[0][1])
    for condition, value in options:
        result = jnp.where(condition, value, result)
    return result


def local(probe_wave, propagator, object_slices, positions, intensities):
    window_size = probe_wave.shape[1]
    band_rows = object_slices.shape[2]
    reach = window_size // band_rows
    local_count = positions.shape[0]
    groups = lax.axis_size("scan")
    sections = lax.axis_size("cuts")
    group = lax.axis_index("scan")
    section = lax.axis_index("cuts")
    assert local_count <= sections
    hosts = [(sections - local_count) // 2 + k for k in range(local_count)]
    host_of = jnp.array(hosts, jnp.int32)

    columns_above = [positions[:, 1]] + [
        passed_along(positions, "scan", distance)[:, 1] for distance in range(1, reach + 1)
    ]
    own_band = object_slices[:, 0]
    row_offsets = positions[:, 0] % band_rows

    def pieces_for(distance):
        columns = columns_above[distance]
        return jnp.stack(
            [lax.dynamic_slice_in_dim(own_band, columns[k], window_size, axis=2) for k in range(local_count)]
        )

    stacked = [pieces_for(0)]
    for distance in range(1, reach + 1):
        outgoing = pieces_for(distance).astype(jnp.bfloat16)
        stacked.append(passed_along(outgoing, "scan", -distance).astype(jnp.float32))
    tall = jnp.concatenate(stacked, axis=2)
    windows_here = jnp.stack(
        [
            lax.dynamic_slice_in_dim(tall[k], row_offsets[k], window_size, axis=1)
            for k in range(local_count)
        ]
    )

    hosted = jnp.argmax(host_of == section).astype(jnp.int32)
    arrivals = {}
    for t in range(sections):
        for k in range(local_count):
            if t != hosts[k]:
                arrivals[(k, t)] = lax.ppermute(
                    windows_here[k].astype(jnp.bfloat16), "cuts", [(t, hosts[k])]
                )

    windows = []
    own_window = lax.dynamic_index_in_dim(windows_here, hosted, 0, keepdims=False)
    for t in range(sections):
        options = [(section == t, own_window)]
        for k in range(local_count):
            if t != hosts[k]:
                options.append(((hosted == k) & (section != t), arrivals[(k, t)].astype(jnp.float32)))
        windows.append(chosen(options))

    transform = lax.optimization_barrier(dft_table(window_size))
    measured = lax.dynamic_index_in_dim(intensities, hosted, 0, keepdims=False)
    grads = whole_chain(probe_wave, propagator, windows, measured, transform)

    returned = {}
    for t in range(sections - 1, -1, -1):
        for k in range(local_count):
            if t != hosts[k]:
                returned[(k, t)] = lax.ppermute(
                    grads[t].astype(jnp.bfloat16), "cuts", [(hosts[k], t)]
                )

    own_grad = chosen([(section == t, grads[t]) for t in range(sections)])
    window_grads = []
    for k in range(local_count):
        options = [(section == hosts[k], own_grad)]
        for t in range(sections):
            if t != hosts[k]:
                options.append((section == t, returned[(k, t)].astype(jnp.float32)))
        window_grads.append(chosen(options))

    width = own_band.shape[2]
    margin = width - window_size

    def placed(piece, column):
        wide = jnp.pad(piece, ((0, 0), (0, 0), (margin, margin)))
        return lax.dynamic_slice_in_dim(wide, margin - column, width, axis=2)

    tall_grads = [
        jnp.pad(window_grads[k], ((0, 0), (band_rows, band_rows), (0, 0))) for k in range(local_count)
    ]

    def band_piece(k, distance):
        start = band_rows + distance * band_rows - row_offsets[k]
        return lax.dynamic_slice_in_dim(tall_grads[k], start, band_rows, axis=1)

    contributions = [placed(band_piece(k, 0), columns_above[0][k]) for k in range(local_count)]
    for distance in range(1, reach + 1):
        outgoing = jnp.stack([band_piece(k, distance) for k in range(local_count)]).astype(jnp.bfloat16)
        incoming = passed_along(outgoing, "scan", distance).astype(jnp.float32)
        contributions += [placed(incoming[k], columns_above[distance][k]) for k in range(local_count)]
    summed = contributions[0]
    for term in contributions[1:]:
        summed = summed + term
    return summed[:, None]


def solution(mesh):
    in_specs = (P(), P(), P(None, "cuts", "scan", None), P("scan", None), P("scan", None, None))
    out_specs = P(None, "cuts", "scan", None)
    return jax.shard_map(local, mesh=mesh, in_specs=in_specs, out_specs=out_specs, check_vma=False)
```
